32 devices in a mesh: groups: 2 (over y), pix: 4 (over z), sub: 2 (over x), inner: 2 (over core).
Axes of the slice: x: 2, y: 2, z: 4, core: 2. Of those that a mesh axis runs over, the one named last changes fastest.
Arguments:
- cube: bfloat16 [20480, 256], P(('groups', 'pix', 'sub', 'inner')), parts along dimension 0, may hold values from -70 to 70
Outputs:
- spectra: bfloat16 [256, 16, 1280], P(('pix', 'sub'), 'groups', 'inner'), parts along dimension 1
The draws below stay inside these ranges and needn't reach their ends.
There are 2 independent parts, one for each index of `groups`. The reference program is written for one: setup_inputs(seed, part) draws one part's arguments, and reference() takes and returns one part's arrays. A program takes and returns all parts, laid end to end along the dimension named above; each array names one. Nothing has to cross between parts.
All inputs are finite; a program needn't handle non-finite values.
Results may differ from the reference program's by a relative error of at most 0.0067.
Values may be sent and summed in bfloat16 or wider, within the bound.
No kernel may reach another device: no remote copies, remote signals or barrier semaphores. Data moves between devices by JAX's collectives and lax.ppermute only.
A program may use at most 64 MiB of HBM per device.

```python
import math
import jax
import jax.numpy as jnp
from jax import lax

NCH = 256
MODES = 32
ITERS = 4
BLOCK = 1280
ROWS = 8
NPIX = 10240


def draw_cube(key, part):
    subkeys = jax.random.split(key, 3)
    position = (jnp.arange(NPIX, dtype=jnp.float32) / NPIX)[:, None]
    chan_scale = jnp.exp(jax.random.uniform(subkeys[1], (1, NCH), minval=0.0, maxval=0.7))
    slopes = jax.random.uniform(subkeys[2], (1, NCH), minval=-1.1, maxval=1.1)
    envelope = chan_scale * jnp.exp(position * slopes + 0.55 * position)
    values = jnp.clip(jax.random.normal(subkeys[0], (NPIX, NCH)), -5.0, 5.0) * envelope
    return (0.5 * values).astype(jnp.bfloat16)


def setup_inputs(seed: int = 0, part: int = 0) -> dict:
    seeds = jax.random.split(jax.random.key(seed), 2)
    part_splits = jax.random.split(jax.random.fold_in(seeds[1], part), 2)
    return {
        "cube": draw_cube(jax.random.fold_in(jax.random.fold_in(seeds[1], part), 71), part),
    }


def matmul_high(left, right):
    return jnp.dot(left, right, precision=lax.Precision.HIGHEST)

def leading_modes(gram_matrix, width_count, sweeps):
    mode_basis = jnp.eye(gram_matrix.shape[0], width_count, dtype=jnp.float32)
    for iteration in range(sweeps):
        product = matmul_high(gram_matrix, mode_basis)
        cross_gram = matmul_high(product.T, product)
        lower_factor = jnp.linalg.cholesky(cross_gram)
        mode_basis = jax.scipy.linalg.solve_triangular(lower_factor, product.T, lower=True).T
    return mode_basis

def delay_table(channels):
    middle = channels // 2
    row_index = lax.broadcasted_iota(jnp.int32, (channels, channels), 0)
    col_index = lax.broadcasted_iota(jnp.int32, (channels, channels), 1)
    harmonic = jnp.where(row_index <= middle, row_index, row_index - middle)
    angles = (harmonic * col_index % channels).astype(jnp.float32) * (2.0 * math.pi / channels)
    values = jnp.where(row_index <= middle, jnp.cos(angles), jnp.sin(angles)) / math.sqrt(channels)
    return values.astype(jnp.bfloat16)

def reference(cube):
    pieces = cube.reshape(ROWS, BLOCK, NCH)

    def accumulate(running, piece):
        partial_gram = lax.dot_general(piece.astype(jnp.float32), piece.astype(jnp.float32), (((0,), (0,)), ((), ())), preferred_element_type=jnp.float32)
        return (running + partial_gram, None)
    gram_matrix, unused = lax.scan(accumulate, jnp.zeros((NCH, NCH), jnp.float32), pieces)
    gram_matrix = gram_matrix / NPIX
    mode_basis = leading_modes(gram_matrix, MODES, ITERS)
    modes_b = mode_basis.astype(jnp.bfloat16)
    table_b = delay_table(NCH)

    def spectra_of(piece):
        amplitudes = jnp.dot(piece.astype(jnp.float32), modes_b.astype(jnp.float32), preferred_element_type=jnp.float32).astype(jnp.bfloat16)
        cleaned = (piece - jnp.dot(amplitudes.astype(jnp.float32), modes_b.T.astype(jnp.float32), preferred_element_type=jnp.float32)).astype(jnp.bfloat16)
        return lax.dot_general(table_b.astype(jnp.float32), cleaned.astype(jnp.float32), (((1,), (1,)), ((), ())), preferred_element_type=jnp.float32).astype(jnp.bfloat16)
    by_rows = lax.map(spectra_of, pieces)
    return jnp.transpose(by_rows, (1, 0, 2))
```

```python
import math

import jax
import jax.numpy as jnp
from jax import lax
from jax.sharding import PartitionSpec as P

MODES = 32
ITERS = 4
VARIANT = "symbutterfly"


def matmul_high(left, right):
    return jnp.dot(left, right, precision=lax.Precision.HIGHEST)


def leading_modes(gram_matrix, width_count, sweeps):
    mode_basis = jnp.eye(gram_matrix.shape[0], width_count, dtype=jnp.float32)
    for iteration in range(sweeps):
        product = matmul_high(gram_matrix, mode_basis)
        cross_gram = matmul_high(product.T, product)
        lower_factor = jnp.linalg.cholesky(cross_gram)
        mode_basis = jax.scipy.linalg.solve_triangular(lower_factor, product.T, lower=True).T
    return mode_basis


def delay_table(channels):
    middle = channels // 2
    row_index = lax.broadcasted_iota(jnp.int32, (channels, channels), 0)
    col_index = lax.broadcasted_iota(jnp.int32, (channels, channels), 1)
    harmonic = jnp.where(row_index <= middle, row_index, row_index - middle)
    angles = (harmonic * col_index % channels).astype(jnp.float32) * (2.0 * math.pi / channels)
    values = jnp.where(row_index <= middle, jnp.cos(angles), jnp.sin(angles)) / math.sqrt(channels)
    return values.astype(jnp.bfloat16)


def steps_of(sizes):
    out = []
    for name, n in sizes:
        d = 1
        while d < n:
            out.append((name, n, d))
            d *= 2
    return out


def butterfly_sum(x, sizes):
    for name, n, d in steps_of(sizes):
        x = x + lax.ppermute(x, name, [(i, i ^ d) for i in range(n)])
    return x


def halving_sum(x, sizes):
    steps = steps_of(sizes)
    for name, n, d in steps:
        bit = (lax.axis_index(name) // d) % 2
        half = x.shape[0] // 2
        lo, hi = x[:half], x[half:]
        send = jnp.where(bit == 0, hi, lo)
        keep = jnp.where(bit == 0, lo, hi)
        x = keep + lax.ppermute(send, name, [(i, i ^ d) for i in range(n)])
    for name, n, d in reversed(steps):
        bit = (lax.axis_index(name) // d) % 2
        other = lax.ppermute(x, name, [(i, i ^ d) for i in range(n)])
        x = jnp.where(bit == 0, jnp.concatenate([x, other]), jnp.concatenate([other, x]))
    return x


def make_local(sizes):
    def reduce(g):
        if VARIANT == "psum":
            return lax.psum(g, ("pix", "sub", "inner"))
        if VARIANT == "butterfly":
            return butterfly_sum(g, sizes)
        if VARIANT == "halving":
            return halving_sum(g, sizes)
        if VARIANT == "symbutterfly":
            h = g.shape[0] // 2
            packed = jnp.concatenate([g[:h, :h], g[:h, h:], g[h:, h:]], axis=0)
            packed = butterfly_sum(packed, sizes)
            a, b, d = packed[:h], packed[h:2 * h], packed[2 * h:]
            return jnp.concatenate([jnp.concatenate([a, b], 1), jnp.concatenate([b.T, d], 1)], 0)
        raise ValueError(VARIANT)

    def local(cube):
        pixels, channels = cube.shape
        pixel_count = pixels * lax.axis_size(("pix", "sub", "inner"))
        partial_gram = lax.dot_general(
            cube, cube, (((0,), (0,)), ((), ())), preferred_element_type=jnp.float32
        )
        gram_matrix = reduce(partial_gram)
        gram_matrix = gram_matrix / pixel_count
        mode_basis = leading_modes(gram_matrix, MODES, ITERS)
        modes_b = mode_basis.astype(jnp.bfloat16)
        amplitudes = jnp.dot(cube, modes_b, preferred_element_type=jnp.float32).astype(jnp.bfloat16)
        cleaned = (cube - jnp.dot(amplitudes, modes_b.T, preferred_element_type=jnp.float32)).astype(
            jnp.bfloat16
        )
        table_b = delay_table(channels)
        coefficients = lax.dot_general(
            table_b, cleaned, (((1,), (1,)), ((), ())), preferred_element_type=jnp.float32
        ).astype(jnp.bfloat16)
        spectra = lax.all_to_all(
            coefficients[:, None, :], ("pix", "sub"), split_axis=0, concat_axis=1, tiled=True
        )
        return spectra
    return local


def solution(mesh):
    sizes = [(a, mesh.shape[a]) for a in ("inner", "sub", "pix")]
    return jax.shard_map(
        make_local(sizes),
        mesh=mesh,
        in_specs=(P(("groups", "pix", "sub", "inner"), None),),
        out_specs=P(("pix", "sub"), "groups", "inner"),
        check_vma=False,
    )
```

```python
import math

import jax
import jax.numpy as jnp
from jax import lax
from jax.experimental import pallas as pl
from jax.experimental.pallas import tpu as pltpu
from jax.sharding import PartitionSpec as P

MODES = 32
ITERS = 4
VARIANT = "symbutterfly"
HI = lax.Precision.HIGHEST


def modes_kernel(g_ref, out_ref):
    g = g_ref[...]
    m = out_ref.shape[0]
    rows = lax.broadcasted_iota(jnp.int32, (m, 1), 0)
    cols = lax.broadcasted_iota(jnp.int32, (1, m), 1)
    xt = g[:m, :]
    for it in range(ITERS):
        pt = xt if it == 0 else jnp.dot(xt, g, precision=HI, preferred_element_type=jnp.float32)
        c = lax.dot_general(pt, pt, (((1,), (1,)), ((), ())), precision=HI,
                            preferred_element_type=jnp.float32)
        xt = pt
        for j in range(m):
            d = jnp.sqrt(c[j:j + 1, j:j + 1])
            q = xt[j:j + 1, :] / d
            rcol = jnp.where(rows > j, c[:, j:j + 1] / d, 0.0)
            rrow = jnp.where(cols > j, c[j:j + 1, :] / d, 0.0)
            xt = jnp.where(rows == j, q, xt - rcol * q)
            c = c - rcol * rrow
    out_ref[...] = xt


def leading_modes_t(gram):
    n = gram.shape[0]
    return pl.pallas_call(
        modes_kernel,
        out_shape=jax.ShapeDtypeStruct((MODES, n), jnp.float32),
        in_specs=[pl.BlockSpec(memory_space=pltpu.VMEM)],
        out_specs=pl.BlockSpec(memory_space=pltpu.VMEM),
    )(gram)


def matmul_high(left, right):
    return jnp.dot(left, right, precision=lax.Precision.HIGHEST)


def leading_modes(gram_matrix, width_count, sweeps):
    mode_basis = jnp.eye(gram_matrix.shape[0], width_count, dtype=jnp.float32)
    for iteration in range(sweeps):
        product = matmul_high(gram_matrix, mode_basis)
        cross_gram = matmul_high(product.T, product)
        lower_factor = jnp.linalg.cholesky(cross_gram)
        mode_basis = jax.scipy.linalg.solve_triangular(lower_factor, product.T, lower=True).T
    return mode_basis


def delay_table(channels):
    middle = channels // 2
    row_index = lax.broadcasted_iota(jnp.int32, (channels, channels), 0)
    col_index = lax.broadcasted_iota(jnp.int32, (channels, channels), 1)
    harmonic = jnp.where(row_index <= middle, row_index, row_index - middle)
    angles = (harmonic * col_index % channels).astype(jnp.float32) * (2.0 * math.pi / channels)
    values = jnp.where(row_index <= middle, jnp.cos(angles), jnp.sin(angles)) / math.sqrt(channels)
    return values.astype(jnp.bfloat16)


def steps_of(sizes):
    out = []
    for name, n in sizes:
        d = 1
        while d < n:
            out.append((name, n, d))
            d *= 2
    return out


def butterfly_sum(x, sizes):
    for name, n, d in steps_of(sizes):
        x = x + lax.ppermute(x, name, [(i, i ^ d) for i in range(n)])
    return x


def halving_sum(x, sizes):
    steps = steps_of(sizes)
    for name, n, d in steps:
        bit = (lax.axis_index(name) // d) % 2
        half = x.shape[0] // 2
        lo, hi = x[:half], x[half:]
        send = jnp.where(bit == 0, hi, lo)
        keep = jnp.where(bit == 0, lo, hi)
        x = keep + lax.ppermute(send, name, [(i, i ^ d) for i in range(n)])
    for name, n, d in reversed(steps):
        bit = (lax.axis_index(name) // d) % 2
        other = lax.ppermute(x, name, [(i, i ^ d) for i in range(n)])
        x = jnp.where(bit == 0, jnp.concatenate([x, other]), jnp.concatenate([other, x]))
    return x


def make_local(sizes):
    def reduce(g):
        if VARIANT == "psum":
            return lax.psum(g, ("pix", "sub", "inner"))
        if VARIANT == "butterfly":
            return butterfly_sum(g, sizes)
        if VARIANT == "halving":
            return halving_sum(g, sizes)
        if VARIANT == "symbutterfly":
            h = g.shape[0] // 2
            packed = jnp.concatenate([g[:h, :h], g[:h, h:], g[h:, h:]], axis=0)
            packed = butterfly_sum(packed, sizes)
            a, b, d = packed[:h], packed[h:2 * h], packed[2 * h:]
            return jnp.concatenate([jnp.concatenate([a, b], 1), jnp.concatenate([b.T, d], 1)], 0)
        raise ValueError(VARIANT)

    def local(cube):
        pixels, channels = cube.shape
        pixel_count = pixels * lax.axis_size(("pix", "sub", "inner"))
        partial_gram = lax.dot_general(
            cube, cube, (((0,), (0,)), ((), ())), preferred_element_type=jnp.float32
        )
        gram_matrix = reduce(partial_gram)
        gram_matrix = gram_matrix / pixel_count
        modes_b = leading_modes_t(gram_matrix).T.astype(jnp.bfloat16)
        amplitudes = jnp.dot(cube, modes_b, preferred_element_type=jnp.float32).astype(jnp.bfloat16)
        cleaned = (cube - jnp.dot(amplitudes, modes_b.T, preferred_element_type=jnp.float32)).astype(
            jnp.bfloat16
        )
        table_b = delay_table(channels)
        coefficients = lax.dot_general(
            table_b, cleaned, (((1,), (1,)), ((), ())), preferred_element_type=jnp.float32
        ).astype(jnp.bfloat16)
        spectra = lax.all_to_all(
            coefficients[:, None, :], ("pix", "sub"), split_axis=0, concat_axis=1, tiled=True
        )
        return spectra
    return local


def solution(mesh):
    sizes = [(a, mesh.shape[a]) for a in ("inner", "sub", "pix")]
    return jax.shard_map(
        make_local(sizes),
        mesh=mesh,
        in_specs=(P(("groups", "pix", "sub", "inner"), None),),
        out_specs=P(("pix", "sub"), "groups", "inner"),
        check_vma=False,
    )
```

```python
import math

import jax
import jax.numpy as jnp
from jax import lax
from jax.experimental import pallas as pl
from jax.experimental.pallas import tpu as pltpu
from jax.sharding import PartitionSpec as P

MODES = 32
ITERS = 4
HI = lax.Precision.HIGHEST


def modes_kernel(g_ref, out_ref):
    g = g_ref[...]
    m = out_ref.shape[0]
    rows = lax.broadcasted_iota(jnp.int32, (m, 1), 0)
    cols = lax.broadcasted_iota(jnp.int32, (1, m), 1)
    xt = g[:m, :]
    for it in range(ITERS):
        pt = xt if it == 0 else jnp.dot(xt, g, precision=HI, preferred_element_type=jnp.float32)
        c = lax.dot_general(pt, pt, (((1,), (1,)), ((), ())), precision=HI,
                            preferred_element_type=jnp.float32)
        xt = pt
        for j in range(m):
            d = jnp.sqrt(c[j:j + 1, j:j + 1])
            q = xt[j:j + 1, :] / d
            rcol = jnp.where(rows > j, c[:, j:j + 1] / d, 0.0)
            rrow = jnp.where(cols > j, c[j:j + 1, :] / d, 0.0)
            xt = jnp.where(rows == j, q, xt - rcol * q)
            c = c - rcol * rrow
    out_ref[...] = xt


def leading_modes_t(gram):
    n = gram.shape[0]
    return pl.pallas_call(
        modes_kernel,
        out_shape=jax.ShapeDtypeStruct((MODES, n), jnp.float32),
        in_specs=[pl.BlockSpec(memory_space=pltpu.VMEM)],
        out_specs=pl.BlockSpec(memory_space=pltpu.VMEM),
    )(gram)


def delay_table(channels):
    middle = channels // 2
    row_index = lax.broadcasted_iota(jnp.int32, (channels, channels), 0)
    col_index = lax.broadcasted_iota(jnp.int32, (channels, channels), 1)
    harmonic = jnp.where(row_index <= middle, row_index, row_index - middle)
    angles = (harmonic * col_index % channels).astype(jnp.float32) * (2.0 * math.pi / channels)
    values = jnp.where(row_index <= middle, jnp.cos(angles), jnp.sin(angles)) / math.sqrt(channels)
    return values.astype(jnp.bfloat16)


def sym_pack(g):
    h = g.shape[0] // 2
    return jnp.concatenate([g[:h, :h], g[:h, h:], g[h:, h:]], axis=0)


def sym_unpack(packed):
    h = packed.shape[0] // 3
    a, b, d = packed[:h], packed[h:2 * h], packed[2 * h:]
    return jnp.concatenate([jnp.concatenate([a, b], 1), jnp.concatenate([b.T, d], 1)], 0)


def xor_perm(n, d):
    return [(i, i ^ d) for i in range(n)]


def halve(x, name, n, d):
    bit = (lax.axis_index(name) // d) % 2
    half = x.shape[0] // 2
    lo, hi = x[:half], x[half:]
    send = jnp.where(bit == 0, hi, lo)
    keep = jnp.where(bit == 0, lo, hi)
    return keep + lax.ppermute(send, name, xor_perm(n, d))


def double(x, name, n, d):
    bit = (lax.axis_index(name) // d) % 2
    other = lax.ppermute(x, name, xor_perm(n, d))
    return jnp.where(bit == 0, jnp.concatenate([x, other]), jnp.concatenate([other, x]))


def butterfly_sum(x, sizes):
    for name, n in sizes:
        d = 1
        while d < n:
            x = x + lax.ppermute(x, name, xor_perm(n, d))
            d *= 2
    return x


def gram_sum(g, mesh):
    n_in = mesh.shape["inner"]
    x = sym_pack(g)
    if n_in == 2:
        x = halve(x, "inner", 2, 1)
        x = butterfly_sum(x, [("sub", mesh.shape["sub"]), ("pix", mesh.shape["pix"])])
        x = double(x, "inner", 2, 1)
    else:
        x = butterfly_sum(x, [(a, mesh.shape[a]) for a in ("inner", "sub", "pix")])
    return sym_unpack(x)


def make_local(mesh):
    def local(cube):
        pixels, channels = cube.shape
        pixel_count = pixels * lax.axis_size(("pix", "sub", "inner"))
        partial_gram = lax.dot_general(
            cube, cube, (((0,), (0,)), ((), ())), preferred_element_type=jnp.float32
        )
        gram_matrix = gram_sum(partial_gram, mesh) / pixel_count
        modes_b = leading_modes_t(gram_matrix).T.astype(jnp.bfloat16)
        amplitudes = jnp.dot(cube, modes_b, preferred_element_type=jnp.float32).astype(jnp.bfloat16)
        cleaned = (cube - jnp.dot(amplitudes, modes_b.T, preferred_element_type=jnp.float32)).astype(
            jnp.bfloat16
        )
        table_b = delay_table(channels)
        coefficients = lax.dot_general(
            table_b, cleaned, (((1,), (1,)), ((), ())), preferred_element_type=jnp.float32
        ).astype(jnp.bfloat16)
        return lax.all_to_all(
            coefficients[:, None, :], ("pix", "sub"), split_axis=0, concat_axis=1, tiled=True
        )
    return local


def solution(mesh):
    return jax.shard_map(
        make_local(mesh),
        mesh=mesh,
        in_specs=(P(("groups", "pix", "sub", "inner"), None),),
        out_specs=P(("pix", "sub"), "groups", "inner"),
        check_vma=False,
    )
```

```python
import math

import jax
import jax.numpy as jnp
from jax import lax
from jax.experimental import pallas as pl
from jax.experimental.pallas import tpu as pltpu
from jax.sharding import PartitionSpec as P

MODES = 32
ITERS = 4
HI = lax.Precision.HIGHEST


def modes_kernel(g_ref, out_ref):
    g = g_ref[...]
    m = out_ref.shape[0]
    rows = lax.broadcasted_iota(jnp.int32, (m, 1), 0)
    cols = lax.broadcasted_iota(jnp.int32, (1, m), 1)
    xt = g[:m, :]
    for it in range(ITERS):
        pt = xt if it == 0 else jnp.dot(xt, g, precision=HI, preferred_element_type=jnp.float32)
        c = lax.dot_general(pt, pt, (((1,), (1,)), ((), ())), precision=HI,
                            preferred_element_type=jnp.float32)
        xt = pt
        for j in range(m):
            d = jnp.sqrt(c[j:j + 1, j:j + 1])
            q = xt[j:j + 1, :] / d
            rcol = jnp.where(rows > j, c[:, j:j + 1] / d, 0.0)
            rrow = jnp.where(cols > j, c[j:j + 1, :] / d, 0.0)
            xt = jnp.where(rows == j, q, xt - rcol * q)
            c = c - rcol * rrow
    out_ref[...] = xt


def leading_modes_t(gram):
    n = gram.shape[0]
    return pl.pallas_call(
        modes_kernel,
        out_shape=jax.ShapeDtypeStruct((MODES, n), jnp.float32),
        in_specs=[pl.BlockSpec(memory_space=pltpu.VMEM)],
        out_specs=pl.BlockSpec(memory_space=pltpu.VMEM),
    )(gram)


def delay_table(channels):
    middle = channels // 2
    row_index = lax.broadcasted_iota(jnp.int32, (channels, channels), 0)
    col_index = lax.broadcasted_iota(jnp.int32, (channels, channels), 1)
    harmonic = jnp.where(row_index <= middle, row_index, row_index - middle)
    angles = (harmonic * col_index % channels).astype(jnp.float32) * (2.0 * math.pi / channels)
    values = jnp.where(row_index <= middle, jnp.cos(angles), jnp.sin(angles)) / math.sqrt(channels)
    return values.astype(jnp.bfloat16)


def sym_pack(g):
    h = g.shape[0] // 2
    return jnp.concatenate([g[:h, :h], g[:h, h:], g[h:, h:]], axis=0)


def sym_unpack(packed):
    h = packed.shape[0] // 3
    a, b, d = packed[:h], packed[h:2 * h], packed[2 * h:]
    return jnp.concatenate([jnp.concatenate([a, b], 1), jnp.concatenate([b.T, d], 1)], 0)


def xor_perm(n, d):
    return [(i, i ^ d) for i in range(n)]


def halve(x, name, n, d):
    bit = (lax.axis_index(name) // d) % 2
    half = x.shape[0] // 2
    lo, hi = x[:half], x[half:]
    send = jnp.where(bit == 0, hi, lo)
    keep = jnp.where(bit == 0, lo, hi)
    return keep + lax.ppermute(send, name, xor_perm(n, d))


def double(x, name, n, d):
    bit = (lax.axis_index(name) // d) % 2
    other = lax.ppermute(x, name, xor_perm(n, d))
    return jnp.where(bit == 0, jnp.concatenate([x, other]), jnp.concatenate([other, x]))


def butterfly_sum(x, sizes):
    for name, n in sizes:
        d = 1
        while d < n:
            x = x + lax.ppermute(x, name, xor_perm(n, d))
            d *= 2
    return x


def gram_sum(g, mesh):
    n_in = mesh.shape["inner"]
    x = sym_pack(g)
    if n_in == 2:
        x = halve(x, "inner", 2, 1)
        x = butterfly_sum(x, [("sub", mesh.shape["sub"]), ("pix", mesh.shape["pix"])])
        x = double(x, "inner", 2, 1)
    else:
        x = butterfly_sum(x, [(a, mesh.shape[a]) for a in ("inner", "sub", "pix")])
    return sym_unpack(x)


def make_local(mesh):
    def local(cube):
        pixels, channels = cube.shape
        pixel_count = pixels * lax.axis_size(("pix", "sub", "inner"))
        partial_gram = lax.dot_general(
            cube, cube, (((0,), (0,)), ((), ())), preferred_element_type=jnp.float32
        )
        gram_matrix = gram_sum(partial_gram, mesh) / pixel_count
        modes_b = leading_modes_t(gram_matrix).T.astype(jnp.bfloat16)
        amplitudes = jnp.dot(cube, modes_b, preferred_element_type=jnp.float32).astype(jnp.bfloat16)
        cleaned = (cube - jnp.dot(amplitudes, modes_b.T, preferred_element_type=jnp.float32)).astype(
            jnp.bfloat16
        )
        table_b = delay_table(channels)
        coefficients = lax.dot_general(
            table_b, cleaned, (((1,), (1,)), ((), ())), preferred_element_type=jnp.float32
        ).astype(jnp.bfloat16)
        k = lax.axis_size(("pix", "sub"))
        blocks = coefficients.reshape(k, coefficients.shape[0] // k, coefficients.shape[1])
        blocks = lax.all_to_all(blocks, ("pix", "sub"), split_axis=0, concat_axis=0, tiled=True)
        return jnp.transpose(blocks, (1, 0, 2))
    return local


def solution(mesh):
    return jax.shard_map(
        make_local(mesh),
        mesh=mesh,
        in_specs=(P(("groups", "pix", "sub", "inner"), None),),
        out_specs=P(("pix", "sub"), "groups", "inner"),
        check_vma=False,
    )
```

```python
import math

import jax
import jax.numpy as jnp
from jax import lax
from jax.experimental import pallas as pl
from jax.experimental.pallas import tpu as pltpu
from jax.sharding import PartitionSpec as P

MODES = 32
ITERS = 4
HI = lax.Precision.HIGHEST


def modes_kernel(g_ref, out_ref):
    g = g_ref[...]
    m = out_ref.shape[0]
    rows = lax.broadcasted_iota(jnp.int32, (m, 1), 0)
    cols = lax.broadcasted_iota(jnp.int32, (1, m), 1)
    xt = g[:m, :]
    for it in range(ITERS):
        pt = xt if it == 0 else jnp.dot(xt, g, precision=HI, preferred_element_type=jnp.float32)
        c = lax.dot_general(pt, pt, (((1,), (1,)), ((), ())), precision=HI,
                            preferred_element_type=jnp.float32)
        xt = pt
        for j in range(m):
            d = jnp.sqrt(c[j:j + 1, j:j + 1])
            q = xt[j:j + 1, :] / d
            rcol = jnp.where(rows > j, c[:, j:j + 1] / d, 0.0)
            rrow = jnp.where(cols > j, c[j:j + 1, :] / d, 0.0)
            xt = jnp.where(rows == j, q, xt - rcol * q)
            c = c - rcol * rrow
    out_ref[...] = xt


def leading_modes_t(gram):
    n = gram.shape[0]
    return pl.pallas_call(
        modes_kernel,
        out_shape=jax.ShapeDtypeStruct((MODES, n), jnp.float32),
        in_specs=[pl.BlockSpec(memory_space=pltpu.VMEM)],
        out_specs=pl.BlockSpec(memory_space=pltpu.VMEM),
    )(gram)


def delay_table(channels):
    middle = channels // 2
    row_index = lax.broadcasted_iota(jnp.int32, (channels, channels), 0)
    col_index = lax.broadcasted_iota(jnp.int32, (channels, channels), 1)
    harmonic = jnp.where(row_index <= middle, row_index, row_index - middle)
    angles = (harmonic * col_index % channels).astype(jnp.float32) * (2.0 * math.pi / channels)
    values = jnp.where(row_index <= middle, jnp.cos(angles), jnp.sin(angles)) / math.sqrt(channels)
    return values.astype(jnp.bfloat16)


def sym_pack(g):
    h = g.shape[0] // 2
    return jnp.concatenate([g[:h, :h], g[:h, h:], g[h:, h:]], axis=0)


def sym_unpack(packed):
    h = packed.shape[0] // 3
    a, b, d = packed[:h], packed[h:2 * h], packed[2 * h:]
    return jnp.concatenate([jnp.concatenate([a, b], 1), jnp.concatenate([b.T, d], 1)], 0)


def xor_perm(n, d):
    return [(i, i ^ d) for i in range(n)]


def halve(x, name, n, d):
    bit = (lax.axis_index(name) // d) % 2
    half = x.shape[0] // 2
    lo, hi = x[:half], x[half:]
    send = jnp.where(bit == 0, hi, lo)
    keep = jnp.where(bit == 0, lo, hi)
    return keep + lax.ppermute(send, name, xor_perm(n, d))


def double(x, name, n, d):
    bit = (lax.axis_index(name) // d) % 2
    other = lax.ppermute(x, name, xor_perm(n, d))
    return jnp.where(bit == 0, jnp.concatenate([x, other]), jnp.concatenate([other, x]))


def butterfly_sum(x, sizes):
    for name, n in sizes:
        d = 1
        while d < n:
            x = x + lax.ppermute(x, name, xor_perm(n, d))
            d *= 2
    return x


def butterfly_steps(sizes):
    steps = []
    for name, n in sizes:
        d = 1
        while d < n:
            steps.append((name, n, d))
            d *= 2
    return steps


def paired_round(x, first, second, order):
    (a1, n1, d1), (a2, n2, d2) = first, second
    r1 = lax.ppermute(x, a1, xor_perm(n1, d1))
    r2 = lax.ppermute(x, a2, xor_perm(n2, d2))
    if a1 == a2:
        r12 = lax.ppermute(x, a1, xor_perm(n1, d1 | d2))
    else:
        if order.index(a1) > order.index(a2):
            a1, n1, d1, a2, n2, d2 = a2, n2, d2, a1, n1, d1
        pairs = [(i * n2 + k, (i ^ d1) * n2 + (k ^ d2)) for i in range(n1) for k in range(n2)]
        r12 = lax.ppermute(x, (a1, a2), pairs)
    return (x + r1) + (r2 + r12)


def gram_sum(g, mesh):
    n_in = mesh.shape["inner"]
    x = sym_pack(g)
    if n_in == 2:
        x = halve(x, "inner", 2, 1)
        steps = butterfly_steps([("sub", mesh.shape["sub"]), ("pix", mesh.shape["pix"])])
        if len(steps) >= 2:
            x = paired_round(x, steps[0], steps[1], list(mesh.axis_names))
            steps = steps[2:]
        for name, n, d in steps:
            x = x + lax.ppermute(x, name, xor_perm(n, d))
        x = double(x, "inner", 2, 1)
    else:
        x = butterfly_sum(x, [(a, mesh.shape[a]) for a in ("inner", "sub", "pix")])
    return sym_unpack(x)


def make_local(mesh):
    def local(cube):
        pixels, channels = cube.shape
        pixel_count = pixels * lax.axis_size(("pix", "sub", "inner"))
        partial_gram = lax.dot_general(
            cube, cube, (((0,), (0,)), ((), ())), preferred_element_type=jnp.float32
        )
        gram_matrix = gram_sum(partial_gram, mesh) / pixel_count
        modes_b = leading_modes_t(gram_matrix).T.astype(jnp.bfloat16)
        amplitudes = jnp.dot(cube, modes_b, preferred_element_type=jnp.float32).astype(jnp.bfloat16)
        cleaned = (cube - jnp.dot(amplitudes, modes_b.T, preferred_element_type=jnp.float32)).astype(
            jnp.bfloat16
        )
        table_b = delay_table(channels)
        coefficients = lax.dot_general(
            table_b, cleaned, (((1,), (1,)), ((), ())), preferred_element_type=jnp.float32
        ).astype(jnp.bfloat16)
        k = lax.axis_size(("pix", "sub"))
        blocks = coefficients.reshape(k, coefficients.shape[0] // k, coefficients.shape[1])
        blocks = lax.all_to_all(blocks, ("pix", "sub"), split_axis=0, concat_axis=0, tiled=True)
        return jnp.transpose(blocks, (1, 0, 2))
    return local


def solution(mesh):
    return jax.shard_map(
        make_local(mesh),
        mesh=mesh,
        in_specs=(P(("groups", "pix", "sub", "inner"), None),),
        out_specs=P(("pix", "sub"), "groups", "inner"),
        check_vma=False,
    )
```

```python
import math

import jax
import ml_dtypes
import numpy as np
import jax.numpy as jnp
from jax import lax
from jax.experimental import pallas as pl
from jax.experimental.pallas import tpu as pltpu
from jax.sharding import PartitionSpec as P

MODES = 32
ITERS = 4
HI = lax.Precision.HIGHEST


def spectra_kernel(g_ref, cube_ref, table_ref, out_ref):
    g = g_ref[...]
    m = MODES
    rows = lax.broadcasted_iota(jnp.int32, (m, 1), 0)
    cols = lax.broadcasted_iota(jnp.int32, (1, m), 1)
    xt = g[:m, :]
    for it in range(ITERS):
        pt = xt if it == 0 else jnp.dot(xt, g, precision=HI, preferred_element_type=jnp.float32)
        c = lax.dot_general(pt, pt, (((1,), (1,)), ((), ())), precision=HI,
                            preferred_element_type=jnp.float32)
        xt = pt
        for j in range(m):
            d = jnp.sqrt(c[j:j + 1, j:j + 1])
            q = xt[j:j + 1, :] / d
            rcol = jnp.where(rows > j, c[:, j:j + 1] / d, 0.0)
            rrow = jnp.where(cols > j, c[j:j + 1, :] / d, 0.0)
            xt = jnp.where(rows == j, q, xt - rcol * q)
            c = c - rcol * rrow
    modes_t = xt.astype(jnp.bfloat16)
    cube = cube_ref[...]
    nt = (((1,), (1,)), ((), ()))
    amplitudes = lax.dot_general(cube, modes_t, nt, preferred_element_type=jnp.float32)
    foreground = jnp.dot(amplitudes.astype(jnp.bfloat16), modes_t, preferred_element_type=jnp.float32)
    cleaned = (cube.astype(jnp.float32) - foreground).astype(jnp.bfloat16)
    coefficients = lax.dot_general(table_ref[...], cleaned, nt, preferred_element_type=jnp.float32)
    out_ref[...] = coefficients.astype(out_ref.dtype)


def spectra_of(gram, cube, table):
    vmem = pl.BlockSpec(memory_space=pltpu.VMEM)
    return pl.pallas_call(
        spectra_kernel,
        out_shape=jax.ShapeDtypeStruct((table.shape[0], cube.shape[0]), jnp.bfloat16),
        in_specs=[vmem, vmem, vmem],
        out_specs=vmem,
    )(gram, cube, table)


def delay_table(channels):
    middle = channels // 2
    row_index = np.arange(channels, dtype=np.int32)[:, None]
    col_index = np.arange(channels, dtype=np.int32)[None, :]
    harmonic = np.where(row_index <= middle, row_index, row_index - middle)
    angles = ((harmonic * col_index) % channels).astype(np.float32) * np.float32(2.0 * math.pi / channels)
    values = np.where(row_index <= middle, np.cos(angles), np.sin(angles)) / np.float32(math.sqrt(channels))
    return values.astype(np.float32).astype(ml_dtypes.bfloat16)


def sym_pack(g):
    h = g.shape[0] // 2
    return jnp.concatenate([g[:h, :h], g[:h, h:], g[h:, h:]], axis=0)


def sym_unpack(packed):
    h = packed.shape[0] // 3
    a, b, d = packed[:h], packed[h:2 * h], packed[2 * h:]
    return jnp.concatenate([jnp.concatenate([a, b], 1), jnp.concatenate([b.T, d], 1)], 0)


def xor_perm(n, d):
    return [(i, i ^ d) for i in range(n)]


def halve(x, name, n, d):
    bit = (lax.axis_index(name) // d) % 2
    half = x.shape[0] // 2
    lo, hi = x[:half], x[half:]
    send = jnp.where(bit == 0, hi, lo)
    keep = jnp.where(bit == 0, lo, hi)
    return keep + lax.ppermute(send, name, xor_perm(n, d))


def double(x, name, n, d):
    bit = (lax.axis_index(name) // d) % 2
    other = lax.ppermute(x, name, xor_perm(n, d))
    return jnp.where(bit == 0, jnp.concatenate([x, other]), jnp.concatenate([other, x]))


def butterfly_sum(x, sizes):
    for name, n in sizes:
        d = 1
        while d < n:
            x = x + lax.ppermute(x, name, xor_perm(n, d))
            d *= 2
    return x


def butterfly_steps(sizes):
    steps = []
    for name, n in sizes:
        d = 1
        while d < n:
            steps.append((name, n, d))
            d *= 2
    return steps


def paired_round(x, first, second, order):
    (a1, n1, d1), (a2, n2, d2) = first, second
    r1 = lax.ppermute(x, a1, xor_perm(n1, d1))
    r2 = lax.ppermute(x, a2, xor_perm(n2, d2))
    if a1 == a2:
        r12 = lax.ppermute(x, a1, xor_perm(n1, d1 | d2))
    else:
        if order.index(a1) > order.index(a2):
            a1, n1, d1, a2, n2, d2 = a2, n2, d2, a1, n1, d1
        pairs = [(i * n2 + k, (i ^ d1) * n2 + (k ^ d2)) for i in range(n1) for k in range(n2)]
        r12 = lax.ppermute(x, (a1, a2), pairs)
    return (x + r1) + (r2 + r12)


def gram_sum(g, mesh):
    n_in = mesh.shape["inner"]
    x = sym_pack(g)
    if n_in == 2:
        x = halve(x, "inner", 2, 1)
        steps = butterfly_steps([("sub", mesh.shape["sub"]), ("pix", mesh.shape["pix"])])
        if len(steps) >= 2:
            x = paired_round(x, steps[0], steps[1], list(mesh.axis_names))
            steps = steps[2:]
        for name, n, d in steps:
            x = x + lax.ppermute(x, name, xor_perm(n, d))
        x = double(x, "inner", 2, 1)
    else:
        x = butterfly_sum(x, [(a, mesh.shape[a]) for a in ("inner", "sub", "pix")])
    return sym_unpack(x)


def make_local(mesh):
    def local(cube):
        pixels, channels = cube.shape
        pixel_count = pixels * lax.axis_size(("pix", "sub", "inner"))
        partial_gram = lax.dot_general(
            cube, cube, (((0,), (0,)), ((), ())), preferred_element_type=jnp.float32
        )
        gram_matrix = gram_sum(partial_gram, mesh) / pixel_count
        coefficients = spectra_of(gram_matrix, cube, jnp.asarray(delay_table(channels)))
        k = lax.axis_size(("pix", "sub"))
        blocks = coefficients.reshape(k, coefficients.shape[0] // k, coefficients.shape[1])
        blocks = lax.all_to_all(blocks, ("pix", "sub"), split_axis=0, concat_axis=0, tiled=True)
        return jnp.transpose(blocks, (1, 0, 2))
    return local


def solution(mesh):
    return jax.shard_map(
        make_local(mesh),
        mesh=mesh,
        in_specs=(P(("groups", "pix", "sub", "inner"), None),),
        out_specs=P(("pix", "sub"), "groups", "inner"),
        check_vma=False,
    )
```

```python
import math

import jax
import ml_dtypes
import numpy as np
import jax.numpy as jnp
from jax import lax
from jax.experimental import pallas as pl
from jax.experimental.pallas import tpu as pltpu
from jax.sharding import PartitionSpec as P

MODES = 32
ITERS = 4
HI = lax.Precision.HIGHEST


def spectra_kernel(g_ref, cube_ref, table_ref, out_ref):
    g = g_ref[...]
    m = MODES
    rows = lax.broadcasted_iota(jnp.int32, (m, 1), 0)
    cols = lax.broadcasted_iota(jnp.int32, (1, m), 1)
    xt = g[:m, :]
    for it in range(ITERS):
        pt = xt if it == 0 else jnp.dot(xt, g, precision=HI, preferred_element_type=jnp.float32)
        c = lax.dot_general(pt, pt, (((1,), (1,)), ((), ())), precision=HI,
                            preferred_element_type=jnp.float32)
        xt = pt
        for j in range(m):
            d = jnp.sqrt(c[j:j + 1, j:j + 1])
            q = xt[j:j + 1, :] / d
            rcol = jnp.where(rows > j, c[:, j:j + 1] / d, 0.0)
            rrow = jnp.where(cols > j, c[j:j + 1, :] / d, 0.0)
            xt = jnp.where(rows == j, q, xt - rcol * q)
            c = c - rcol * rrow
    modes_t = xt.astype(jnp.bfloat16)
    cube = cube_ref[...]
    nt = (((1,), (1,)), ((), ()))
    amplitudes = lax.dot_general(cube, modes_t, nt, preferred_element_type=jnp.float32)
    foreground = jnp.dot(amplitudes.astype(jnp.bfloat16), modes_t, preferred_element_type=jnp.float32)
    cleaned = (cube.astype(jnp.float32) - foreground).astype(jnp.bfloat16)
    coefficients = lax.dot_general(table_ref[...], cleaned, nt, preferred_element_type=jnp.float32)
    out_ref[...] = coefficients.astype(out_ref.dtype)


def spectra_of(gram, cube, table):
    vmem = pl.BlockSpec(memory_space=pltpu.VMEM)
    return pl.pallas_call(
        spectra_kernel,
        out_shape=jax.ShapeDtypeStruct((table.shape[0], cube.shape[0]), jnp.bfloat16),
        in_specs=[vmem, vmem, vmem],
        out_specs=vmem,
    )(gram, cube, table)


def delay_table(channels):
    middle = channels // 2
    row_index = np.arange(channels, dtype=np.int32)[:, None]
    col_index = np.arange(channels, dtype=np.int32)[None, :]
    harmonic = np.where(row_index <= middle, row_index, row_index - middle)
    angles = ((harmonic * col_index) % channels).astype(np.float32) * np.float32(2.0 * math.pi / channels)
    values = np.where(row_index <= middle, np.cos(angles), np.sin(angles)) / np.float32(math.sqrt(channels))
    return values.astype(np.float32).astype(ml_dtypes.bfloat16)


def sym_pack(g):
    q = g.shape[0] // 4
    blk = lambda i, j: g[i * q:(i + 1) * q, j * q:(j + 1) * q]
    slabs = [g[0:q, 0:2 * q], g[0:q, 2 * q:4 * q], g[q:2 * q, q:3 * q],
             jnp.concatenate([blk(1, 3), blk(3, 3)], axis=1), g[2 * q:3 * q, 2 * q:4 * q]]
    return jnp.concatenate(slabs, axis=0)


def sym_unpack(packed):
    q = packed.shape[1] // 2
    s = [packed[k * q:(k + 1) * q] for k in range(5)]
    b = {(0, 0): s[0][:, :q], (0, 1): s[0][:, q:], (0, 2): s[1][:, :q], (0, 3): s[1][:, q:],
         (1, 1): s[2][:, :q], (1, 2): s[2][:, q:], (1, 3): s[3][:, :q], (3, 3): s[3][:, q:],
         (2, 2): s[4][:, :q], (2, 3): s[4][:, q:]}
    rows = [jnp.concatenate([b[(i, j)] if i <= j else b[(j, i)].T for j in range(4)], axis=1)
            for i in range(4)]
    return jnp.concatenate(rows, axis=0)


def xor_perm(n, d):
    return [(i, i ^ d) for i in range(n)]


def halve(x, name, n, d):
    bit = (lax.axis_index(name) // d) % 2
    half = x.shape[0] // 2
    lo, hi = x[:half], x[half:]
    send = jnp.where(bit == 0, hi, lo)
    keep = jnp.where(bit == 0, lo, hi)
    return keep + lax.ppermute(send, name, xor_perm(n, d))


def double(x, name, n, d):
    bit = (lax.axis_index(name) // d) % 2
    other = lax.ppermute(x, name, xor_perm(n, d))
    return jnp.where(bit == 0, jnp.concatenate([x, other]), jnp.concatenate([other, x]))


def butterfly_sum(x, sizes):
    for name, n in sizes:
        d = 1
        while d < n:
            x = x + lax.ppermute(x, name, xor_perm(n, d))
            d *= 2
    return x


def butterfly_steps(sizes):
    steps = []
    for name, n in sizes:
        d = 1
        while d < n:
            steps.append((name, n, d))
            d *= 2
    return steps


def paired_round(x, first, second, order):
    (a1, n1, d1), (a2, n2, d2) = first, second
    r1 = lax.ppermute(x, a1, xor_perm(n1, d1))
    r2 = lax.ppermute(x, a2, xor_perm(n2, d2))
    if a1 == a2:
        r12 = lax.ppermute(x, a1, xor_perm(n1, d1 | d2))
    else:
        if order.index(a1) > order.index(a2):
            a1, n1, d1, a2, n2, d2 = a2, n2, d2, a1, n1, d1
        pairs = [(i * n2 + k, (i ^ d1) * n2 + (k ^ d2)) for i in range(n1) for k in range(n2)]
        r12 = lax.ppermute(x, (a1, a2), pairs)
    return (x + r1) + (r2 + r12)


def gram_sum(g, mesh):
    n_in = mesh.shape["inner"]
    x = sym_pack(g)
    if n_in == 2:
        x = halve(x, "inner", 2, 1)
        steps = butterfly_steps([("sub", mesh.shape["sub"]), ("pix", mesh.shape["pix"])])
        if len(steps) >= 2:
            x = paired_round(x, steps[0], steps[1], list(mesh.axis_names))
            steps = steps[2:]
        for name, n, d in steps:
            x = x + lax.ppermute(x, name, xor_perm(n, d))
        x = double(x, "inner", 2, 1)
    else:
        x = butterfly_sum(x, [(a, mesh.shape[a]) for a in ("inner", "sub", "pix")])
    return sym_unpack(x)


def make_local(mesh):
    def local(cube):
        pixels, channels = cube.shape
        pixel_count = pixels * lax.axis_size(("pix", "sub", "inner"))
        partial_gram = lax.dot_general(
            cube, cube, (((0,), (0,)), ((), ())), preferred_element_type=jnp.float32
        )
        gram_matrix = gram_sum(partial_gram, mesh) / pixel_count
        coefficients = spectra_of(gram_matrix, cube, jnp.asarray(delay_table(channels)))
        k = lax.axis_size(("pix", "sub"))
        blocks = coefficients.reshape(k, coefficients.shape[0] // k, coefficients.shape[1])
        blocks = lax.all_to_all(blocks, ("pix", "sub"), split_axis=0, concat_axis=0, tiled=True)
        return jnp.transpose(blocks, (1, 0, 2))
    return local


def solution(mesh):
    return jax.shard_map(
        make_local(mesh),
        mesh=mesh,
        in_specs=(P(("groups", "pix", "sub", "inner"), None),),
        out_specs=P(("pix", "sub"), "groups", "inner"),
        check_vma=False,
    )
```

```python
import math

import jax
import ml_dtypes
import numpy as np
import jax.numpy as jnp
from jax import lax
from jax.experimental import pallas as pl
from jax.experimental.pallas import tpu as pltpu
from jax.sharding import PartitionSpec as P

MODES = 32
ITERS = 4
HI = lax.Precision.HIGHEST


def spectra_kernel(g_ref, cube_ref, table_ref, out_ref):
    g = g_ref[...]
    m = MODES
    rows = lax.broadcasted_iota(jnp.int32, (m, 1), 0)
    cols = lax.broadcasted_iota(jnp.int32, (1, m), 1)
    xt = g[:m, :]
    for it in range(ITERS):
        pt = xt if it == 0 else jnp.dot(xt, g, precision=HI, preferred_element_type=jnp.float32)
        c = lax.dot_general(pt, pt, (((1,), (1,)), ((), ())), precision=HI,
                            preferred_element_type=jnp.float32)
        xt = pt
        for j in range(m):
            d = jnp.sqrt(c[j:j + 1, j:j + 1])
            q = xt[j:j + 1, :] / d
            rcol = jnp.where(rows > j, c[:, j:j + 1] / d, 0.0)
            rrow = jnp.where(cols > j, c[j:j + 1, :] / d, 0.0)
            xt = jnp.where(rows == j, q, xt - rcol * q)
            c = c - rcol * rrow
    modes_t = xt.astype(jnp.bfloat16)
    cube = cube_ref[...]
    nt = (((1,), (1,)), ((), ()))
    amplitudes = lax.dot_general(cube, modes_t, nt, preferred_element_type=jnp.float32)
    foreground = jnp.dot(amplitudes.astype(jnp.bfloat16), modes_t, preferred_element_type=jnp.float32)
    cleaned = (cube.astype(jnp.float32) - foreground).astype(jnp.bfloat16)
    coefficients = lax.dot_general(table_ref[...], cleaned, nt, preferred_element_type=jnp.float32)
    out_ref[...] = coefficients.astype(out_ref.dtype)


def spectra_of(gram, cube, table):
    vmem = pl.BlockSpec(memory_space=pltpu.VMEM)
    return pl.pallas_call(
        spectra_kernel,
        out_shape=jax.ShapeDtypeStruct((table.shape[0], cube.shape[0]), jnp.bfloat16),
        in_specs=[vmem, vmem, vmem],
        out_specs=vmem,
    )(gram, cube, table)


def delay_table(channels):
    middle = channels // 2
    row_index = np.arange(channels, dtype=np.int32)[:, None]
    col_index = np.arange(channels, dtype=np.int32)[None, :]
    harmonic = np.where(row_index <= middle, row_index, row_index - middle)
    angles = ((harmonic * col_index) % channels).astype(np.float32) * np.float32(2.0 * math.pi / channels)
    values = np.where(row_index <= middle, np.cos(angles), np.sin(angles)) / np.float32(math.sqrt(channels))
    return values.astype(np.float32).astype(ml_dtypes.bfloat16)


def sym_pack(g):
    q = g.shape[0] // 4
    slabs = [g[0:q, 0:2 * q], g[0:q, 2 * q:4 * q], g[q:2 * q, 2 * q:4 * q],
             jnp.concatenate([g[q:2 * q, q:2 * q], g[3 * q:4 * q, 3 * q:4 * q]], axis=1),
             g[2 * q:3 * q, 2 * q:4 * q]]
    return jnp.concatenate(slabs, axis=0)


def sym_unpack(packed):
    q = packed.shape[1] // 2
    s = [packed[k * q:(k + 1) * q] for k in range(5)]
    a = jnp.concatenate([s[0], jnp.concatenate([s[0][:, q:].T, s[3][:, :q]], axis=1)], axis=0)
    d = jnp.concatenate([s[4], jnp.concatenate([s[4][:, q:].T, s[3][:, q:]], axis=1)], axis=0)
    b = jnp.concatenate([s[1], s[2]], axis=0)
    return jnp.concatenate([jnp.concatenate([a, b], axis=1), jnp.concatenate([b.T, d], axis=1)], axis=0)


def xor_perm(n, d):
    return [(i, i ^ d) for i in range(n)]


def halve(x, name, n, d):
    bit = (lax.axis_index(name) // d) % 2
    half = x.shape[0] // 2
    lo, hi = x[:half], x[half:]
    send = jnp.where(bit == 0, hi, lo)
    keep = jnp.where(bit == 0, lo, hi)
    return keep + lax.ppermute(send, name, xor_perm(n, d))


def double(x, name, n, d):
    bit = (lax.axis_index(name) // d) % 2
    other = lax.ppermute(x, name, xor_perm(n, d))
    return jnp.where(bit == 0, jnp.concatenate([x, other]), jnp.concatenate([other, x]))


def butterfly_sum(x, sizes):
    for name, n in sizes:
        d = 1
        while d < n:
            x = x + lax.ppermute(x, name, xor_perm(n, d))
            d *= 2
    return x


def butterfly_steps(sizes):
    steps = []
    for name, n in sizes:
        d = 1
        while d < n:
            steps.append((name, n, d))
            d *= 2
    return steps


def paired_round(x, first, second, order):
    (a1, n1, d1), (a2, n2, d2) = first, second
    r1 = lax.ppermute(x, a1, xor_perm(n1, d1))
    r2 = lax.ppermute(x, a2, xor_perm(n2, d2))
    if a1 == a2:
        r12 = lax.ppermute(x, a1, xor_perm(n1, d1 | d2))
    else:
        if order.index(a1) > order.index(a2):
            a1, n1, d1, a2, n2, d2 = a2, n2, d2, a1, n1, d1
        pairs = [(i * n2 + k, (i ^ d1) * n2 + (k ^ d2)) for i in range(n1) for k in range(n2)]
        r12 = lax.ppermute(x, (a1, a2), pairs)
    return (x + r1) + (r2 + r12)


def gram_sum(g, mesh):
    n_in = mesh.shape["inner"]
    x = sym_pack(g)
    if n_in == 2:
        x = halve(x, "inner", 2, 1)
        steps = butterfly_steps([("sub", mesh.shape["sub"]), ("pix", mesh.shape["pix"])])
        if len(steps) >= 2:
            x = paired_round(x, steps[0], steps[1], list(mesh.axis_names))
            steps = steps[2:]
        for name, n, d in steps:
            x = x + lax.ppermute(x, name, xor_perm(n, d))
        x = double(x, "inner", 2, 1)
    else:
        x = butterfly_sum(x, [(a, mesh.shape[a]) for a in ("inner", "sub", "pix")])
    return sym_unpack(x)


def make_local(mesh):
    def local(cube):
        pixels, channels = cube.shape
        pixel_count = pixels * lax.axis_size(("pix", "sub", "inner"))
        partial_gram = lax.dot_general(
            cube, cube, (((0,), (0,)), ((), ())), preferred_element_type=jnp.float32
        )
        gram_matrix = gram_sum(partial_gram, mesh) / pixel_count
        coefficients = spectra_of(gram_matrix, cube, jnp.asarray(delay_table(channels)))
        k = lax.axis_size(("pix", "sub"))
        blocks = coefficients.reshape(k, coefficients.shape[0] // k, coefficients.shape[1])
        blocks = lax.all_to_all(blocks, ("pix", "sub"), split_axis=0, concat_axis=0, tiled=True)
        return jnp.transpose(blocks, (1, 0, 2))
    return local


def solution(mesh):
    return jax.shard_map(
        make_local(mesh),
        mesh=mesh,
        in_specs=(P(("groups", "pix", "sub", "inner"), None),),
        out_specs=P(("pix", "sub"), "groups", "inner"),
        check_vma=False,
    )
```

```python
import math

import jax
import ml_dtypes
import numpy as np
import jax.numpy as jnp
from jax import lax
from jax.experimental import pallas as pl
from jax.experimental.pallas import tpu as pltpu
from jax.sharding import PartitionSpec as P

MODES = 32
ITERS = 4
HI = lax.Precision.HIGHEST


def spectra_kernel(g_ref, cube_hbm, table_hbm, out_ref, cube_ref, table_ref, sems):
    cube_copy = pltpu.make_async_copy(cube_hbm, cube_ref, sems.at[0])
    table_copy = pltpu.make_async_copy(table_hbm, table_ref, sems.at[1])
    cube_copy.start()
    table_copy.start()
    g = g_ref[...]
    m = MODES
    rows = lax.broadcasted_iota(jnp.int32, (m, 1), 0)
    cols = lax.broadcasted_iota(jnp.int32, (1, m), 1)
    xt = g[:m, :]
    for it in range(ITERS):
        pt = xt if it == 0 else jnp.dot(xt, g, precision=HI, preferred_element_type=jnp.float32)
        c = lax.dot_general(pt, pt, (((1,), (1,)), ((), ())), precision=HI,
                            preferred_element_type=jnp.float32)
        xt = pt
        for j in range(m):
            d = jnp.sqrt(c[j:j + 1, j:j + 1])
            q = xt[j:j + 1, :] / d
            rcol = jnp.where(rows > j, c[:, j:j + 1] / d, 0.0)
            rrow = jnp.where(cols > j, c[j:j + 1, :] / d, 0.0)
            xt = jnp.where(rows == j, q, xt - rcol * q)
            c = c - rcol * rrow
    modes_t = xt.astype(jnp.bfloat16)
    cube_copy.wait()
    table_copy.wait()
    cube = cube_ref[...]
    nt = (((1,), (1,)), ((), ()))
    amplitudes = lax.dot_general(cube, modes_t, nt, preferred_element_type=jnp.float32)
    foreground = jnp.dot(amplitudes.astype(jnp.bfloat16), modes_t, preferred_element_type=jnp.float32)
    cleaned = (cube.astype(jnp.float32) - foreground).astype(jnp.bfloat16)
    coefficients = lax.dot_general(table_ref[...], cleaned, nt, preferred_element_type=jnp.float32)
    out_ref[...] = coefficients.astype(out_ref.dtype)


def spectra_of(gram, cube, table):
    vmem = pl.BlockSpec(memory_space=pltpu.VMEM)
    return pl.pallas_call(
        spectra_kernel,
        out_shape=jax.ShapeDtypeStruct((table.shape[0], cube.shape[0]), jnp.bfloat16),
        in_specs=[vmem, pl.BlockSpec(memory_space=pl.ANY), pl.BlockSpec(memory_space=pl.ANY)],
        out_specs=vmem,
        scratch_shapes=[pltpu.VMEM(cube.shape, cube.dtype), pltpu.VMEM(table.shape, table.dtype),
                        pltpu.SemaphoreType.DMA((2,))],
    )(gram, cube, table)


def delay_table(channels):
    middle = channels // 2
    row_index = np.arange(channels, dtype=np.int32)[:, None]
    col_index = np.arange(channels, dtype=np.int32)[None, :]
    harmonic = np.where(row_index <= middle, row_index, row_index - middle)
    angles = ((harmonic * col_index) % channels).astype(np.float32) * np.float32(2.0 * math.pi / channels)
    values = np.where(row_index <= middle, np.cos(angles), np.sin(angles)) / np.float32(math.sqrt(channels))
    return values.astype(np.float32).astype(ml_dtypes.bfloat16)


def sym_pack(g):
    q = g.shape[0] // 4
    slabs = [g[0:q, 0:2 * q], g[0:q, 2 * q:4 * q], g[q:2 * q, 2 * q:4 * q],
             jnp.concatenate([g[q:2 * q, q:2 * q], g[3 * q:4 * q, 3 * q:4 * q]], axis=1),
             g[2 * q:3 * q, 2 * q:4 * q]]
    return jnp.concatenate(slabs, axis=0)


def sym_unpack(packed):
    q = packed.shape[1] // 2
    s = [packed[k * q:(k + 1) * q] for k in range(5)]
    a = jnp.concatenate([s[0], jnp.concatenate([s[0][:, q:].T, s[3][:, :q]], axis=1)], axis=0)
    d = jnp.concatenate([s[4], jnp.concatenate([s[4][:, q:].T, s[3][:, q:]], axis=1)], axis=0)
    b = jnp.concatenate([s[1], s[2]], axis=0)
    return jnp.concatenate([jnp.concatenate([a, b], axis=1), jnp.concatenate([b.T, d], axis=1)], axis=0)


def xor_perm(n, d):
    return [(i, i ^ d) for i in range(n)]


def halve(x, name, n, d):
    bit = (lax.axis_index(name) // d) % 2
    half = x.shape[0] // 2
    lo, hi = x[:half], x[half:]
    send = jnp.where(bit == 0, hi, lo)
    keep = jnp.where(bit == 0, lo, hi)
    return keep + lax.ppermute(send, name, xor_perm(n, d))


def double(x, name, n, d):
    bit = (lax.axis_index(name) // d) % 2
    other = lax.ppermute(x, name, xor_perm(n, d))
    return jnp.where(bit == 0, jnp.concatenate([x, other]), jnp.concatenate([other, x]))


def butterfly_sum(x, sizes):
    for name, n in sizes:
        d = 1
        while d < n:
            x = x + lax.ppermute(x, name, xor_perm(n, d))
            d *= 2
    return x


def butterfly_steps(sizes):
    steps = []
    for name, n in sizes:
        d = 1
        while d < n:
            steps.append((name, n, d))
            d *= 2
    return steps


def paired_round(x, first, second, order):
    (a1, n1, d1), (a2, n2, d2) = first, second
    r1 = lax.ppermute(x, a1, xor_perm(n1, d1))
    r2 = lax.ppermute(x, a2, xor_perm(n2, d2))
    if a1 == a2:
        r12 = lax.ppermute(x, a1, xor_perm(n1, d1 | d2))
    else:
        if order.index(a1) > order.index(a2):
            a1, n1, d1, a2, n2, d2 = a2, n2, d2, a1, n1, d1
        pairs = [(i * n2 + k, (i ^ d1) * n2 + (k ^ d2)) for i in range(n1) for k in range(n2)]
        r12 = lax.ppermute(x, (a1, a2), pairs)
    return (x + r1) + (r2 + r12)


def gram_sum(g, mesh):
    n_in = mesh.shape["inner"]
    x = sym_pack(g)
    if n_in == 2:
        x = halve(x, "inner", 2, 1)
        steps = butterfly_steps([("sub", mesh.shape["sub"]), ("pix", mesh.shape["pix"])])
        if len(steps) >= 2:
            x = paired_round(x, steps[0], steps[1], list(mesh.axis_names))
            steps = steps[2:]
        for name, n, d in steps:
            x = x + lax.ppermute(x, name, xor_perm(n, d))
        x = double(x, "inner", 2, 1)
    else:
        x = butterfly_sum(x, [(a, mesh.shape[a]) for a in ("inner", "sub", "pix")])
    return sym_unpack(x)


def make_local(mesh):
    def local(cube):
        pixels, channels = cube.shape
        pixel_count = pixels * lax.axis_size(("pix", "sub", "inner"))
        partial_gram = lax.dot_general(
            cube, cube, (((0,), (0,)), ((), ())), preferred_element_type=jnp.float32
        )
        gram_matrix = gram_sum(partial_gram, mesh) / pixel_count
        coefficients = spectra_of(gram_matrix, cube, jnp.asarray(delay_table(channels)))
        k = lax.axis_size(("pix", "sub"))
        blocks = coefficients.reshape(k, coefficients.shape[0] // k, coefficients.shape[1])
        blocks = lax.all_to_all(blocks, ("pix", "sub"), split_axis=0, concat_axis=0, tiled=True)
        return jnp.transpose(blocks, (1, 0, 2))
    return local


def solution(mesh):
    return jax.shard_map(
        make_local(mesh),
        mesh=mesh,
        in_specs=(P(("groups", "pix", "sub", "inner"), None),),
        out_specs=P(("pix", "sub"), "groups", "inner"),
        check_vma=False,
    )
```
